256 devices in a mesh: dp: 4 (over y), seq: 16 (over z, core), tensor: 4 (over x).
Axes of the slice: x: 4, y: 4, z: 8, core: 2. Of those that a mesh axis runs over, the one named last changes fastest.
Arguments:
- queries: bfloat16 [16384, 8192], P(('dp', 'seq'), 'tensor'), parts along dimension 0, may hold values from -110 to 110
- keys_values: bfloat16 [16384, 2, 1024], P(('dp', 'seq'), None, 'tensor'), parts along dimension 0, may hold values from -4.5 to 4.5
- out_weight: bfloat16 [8192, 8192], P('tensor', 'seq'), may hold values from -0.1875 to 0.1875
- residual: bfloat16 [16384, 8192], P(('dp', 'tensor'), 'seq'), parts along dimension 0, may hold values from -3 to 3
- segments: int32 [16384], P('dp'), parts along dimension 0, may hold values from 0 to 3, never falling along the last dimension, each value on 1 to 2048 neighbouring positions
Outputs:
- layer_out: bfloat16 [16384, 8192], P(('dp', 'tensor'), 'seq'), parts along dimension 0
The draws below stay inside these ranges and needn't reach their ends.
There are 4 independent parts, one for each index of `dp`. The reference program is written for one: setup_inputs(seed, part) draws one part's arguments, and reference() takes and returns one part's arrays. A program takes and returns all parts, laid end to end along the dimension named above; an argument that names none is the same for every part. Nothing has to cross between parts.
Inputs may be any that keep to these rules, and one draw needn't show every extreme that they name: `segments`: segment numbers never fall along the tokens.
All inputs are finite; a program needn't handle non-finite values.
Results may differ from the reference program's by a relative error of at most 0.0085.
Values may be sent and summed in bfloat16 or wider, within the bound.
No kernel may reach another device: no remote copies, remote signals or barrier semaphores. Data moves between devices by JAX's collectives and lax.ppermute only.
A program may use at most 128 MiB of HBM per device.

```python
import math
import jax
import jax.numpy as jnp
import numpy as np
from jax import lax

D = 8192
H = 64
KVH = 8
HD = 128
L = 4096
SEQS = 1
TOKENS = 4096


def shared_keys(key):
    drawn = jax.random.normal(jax.random.fold_in(key, 11), (TOKENS, 2, KVH * HD), jnp.float32)
    return jnp.clip(drawn, -4.5, 4.5)


def draw_keys_values(key, part):
    drawn = shared_keys(key)
    return drawn.astype(jnp.bfloat16)


def draw_queries(key, part):
    drawn = jax.random.normal(jax.random.fold_in(key, 12), (TOKENS, H * HD), jnp.float32)
    return jnp.clip(1.5 * drawn, -9.0, 9.0).astype(jnp.bfloat16)


def steps_of(rng, dims, cuts, low, largest):
    loudness = 1.0
    for axis_at, shards_of in cuts:
        draws = jax.random.uniform(jax.random.fold_in(jax.random.fold_in(rng, 6), axis_at), (shards_of,), jnp.float32, low / len(cuts), largest / len(cuts))
        loudness = loudness * jnp.repeat(jnp.exp(draws), dims[axis_at] // shards_of).reshape((-1,) + (1,) * (len(dims) - 1 - axis_at))
    return loudness


def profile(number_of, total, limit, skew):
    loads = [(1 << 20) // math.isqrt(grade ** skew) + 1 for grade in range(2, number_of + 1)]
    rest, counts = total - limit - (number_of - 1), [1] * (number_of - 1)
    while rest > 0:
        candidates = [i for i in range(number_of - 1) if counts[i] < limit]
        whole, left = sum([loads[i] for i in candidates]), rest
        for i in candidates:
            addition = min(limit - counts[i], max(1, left * loads[i] // whole), rest)
            counts[i] = counts[i] + addition
            rest = rest - addition
    return np.array([limit] + counts)


def uneven(key, amount, total, reach, slope):
    if amount == 2:
        one = jax.random.randint(key, (), max(1, total - reach), min(reach, total - 1) + 1)
        return jnp.stack([one, total - one])
    sizes = jnp.asarray(profile(amount, total, reach, slope), jnp.int32)
    pairs = (amount - 1) // 2
    donor, taker = sizes[1:1 + 2 * pairs:2], sizes[2:2 + 2 * pairs:2]
    margin = jnp.minimum(donor - 1, reach - taker)
    passed = jax.random.randint(jax.random.fold_in(key, 1), (pairs,), 0, 1 << 20) % (margin + 1)
    sizes = sizes.at[1:1 + 2 * pairs:2].set(donor - passed).at[2:2 + 2 * pairs:2].set(taker + passed)
    return sizes[jax.random.permutation(jax.random.fold_in(key, 2), amount)]


def bell_draw(key, extent, deviation, limit, shards=(), kind=jnp.bfloat16):
    result = deviation * jax.random.normal(key, extent, jnp.float32)
    if shards:
        result = result * steps_of(key, extent, shards, -0.22, 0.18)
    return jnp.clip(result, -limit, limit).astype(kind)


def setup_inputs(seed: int = 0, part: int = 0) -> dict:
    key_of = jax.random.split(jax.random.key(seed), 6)
    part_splits = jax.random.split(jax.random.fold_in(key_of[5], part), 6)
    queries = draw_queries(jax.random.fold_in(jax.random.fold_in(key_of[5], part), 71), part)
    keys_values = draw_keys_values(jax.random.fold_in(jax.random.fold_in(key_of[5], part), 71), part)
    out_weight = bell_draw(key_of[2], (H * HD, D), (H * HD // 8) ** -0.5, 0.1875, ((0, 4), (1, 16)))
    residual = bell_draw(part_splits[3], (TOKENS, D), 0.5, 3.0, ((0, 4), (1, 16)))
    segments = jnp.searchsorted(jnp.cumsum(uneven(part_splits[4], SEQS * 4, TOKENS, L // 2, 2)), jnp.arange(TOKENS), side="right").astype(jnp.int32)
    return dict(queries=queries, keys_values=keys_values, out_weight=out_weight, residual=residual, segments=segments)


def one_head(head, queries, keys_values, segments):
    group_size = H // KVH
    kv_head = head // group_size
    query_head = lax.dynamic_slice_in_dim(queries, head * HD, HD, 1).astype(jnp.float32).reshape(SEQS, L, HD)
    key_head = lax.dynamic_slice_in_dim(keys_values[:, 0, :], kv_head * HD, HD, 1).astype(jnp.float32).reshape(SEQS, L, HD)
    value_head = lax.dynamic_slice_in_dim(keys_values[:, 1, :], kv_head * HD, HD, 1).astype(jnp.float32).reshape(SEQS, L, HD)
    raw_scores = jnp.einsum("sqd,skd->sqk", query_head, key_head) * (HD ** -0.5)
    positions = jnp.arange(L, dtype=jnp.int32)
    causal = positions[None, :] <= positions[:, None]
    doc_ids = segments.reshape(SEQS, L)
    allowed = causal[None, :, :] & (doc_ids[:, :, None] == doc_ids[:, None, :])
    masked = jnp.where(allowed, raw_scores, -1e30)
    highest = jnp.max(masked, axis=-1, keepdims=True)
    exponents = jnp.where(allowed, jnp.exp(masked - highest), 0.0)
    weights = (exponents / jnp.sum(exponents, axis=-1, keepdims=True)).astype(jnp.bfloat16)
    blended = jnp.einsum("sqk,skd->sqd", weights.astype(jnp.float32), value_head)
    return blended.astype(jnp.bfloat16).reshape(SEQS * L, HD)


def reference(queries, keys_values, out_weight, residual, segments):
    stacked = lax.map(lambda head: one_head(head, queries, keys_values, segments), jnp.arange(H, dtype=jnp.int32))
    heads_out = jnp.transpose(stacked, (1, 0, 2)).reshape(SEQS * L, H * HD)
    projected = jnp.dot(heads_out, out_weight, preferred_element_type=jnp.float32)
    return (residual.astype(jnp.float32) + projected).astype(jnp.bfloat16)
```

```python
import jax
import jax.numpy as jnp
import numpy as np
from jax import lax
from jax.sharding import PartitionSpec as P

H = 64
KVH = 8
HD = 128
L = 4096
CHUNKS = 4


def attend_rows(query_head, key_head, value_head, doc_ids, first_row, rows):
    key_end = first_row + rows
    query_block = query_head[first_row:key_end]
    raw_scores = (
        jnp.einsum(
            "qd,kd->qk",
            query_block,
            key_head[:key_end],
            preferred_element_type=jnp.float32,
        )
        * HD ** (-0.5)
    )
    query_pos = first_row + jnp.arange(rows)[:, None]
    key_pos = jnp.arange(key_end)[None, :]
    same_doc = doc_ids[first_row:key_end, None] == doc_ids[None, :key_end]
    allowed = (key_pos <= query_pos) & same_doc
    masked = jnp.where(allowed, raw_scores, -1e30)
    highest = jnp.max(masked, axis=-1, keepdims=True)
    exponents = jnp.where(allowed, jnp.exp(masked - highest), 0.0)
    weights = (exponents / jnp.sum(exponents, axis=-1, keepdims=True)).astype(jnp.bfloat16)
    blended = jnp.einsum(
        "qk,kd->qd", weights, value_head[:key_end], preferred_element_type=jnp.float32
    )
    return blended.astype(jnp.bfloat16)


def on_device(queries, keys_values, out_weight, residual, segments):
    n_seq = lax.axis_size("seq")
    n_ten = lax.axis_size("tensor")
    seq_idx = lax.axis_index("seq")
    tok_dev = queries.shape[0]
    heads_ten = queries.shape[1] // HD
    heads_dev = heads_ten // n_seq
    assert heads_dev == 1
    group_size = H // KVH
    query_slab = queries.reshape(tok_dev, 1, heads_ten * HD)
    query_all = lax.all_to_all(query_slab, "seq", split_axis=2, concat_axis=0, tiled=True)
    query_head = query_all.reshape(query_all.shape[0], HD)
    rows_all = query_head.shape[0]
    assert rows_all == L
    pair_all = lax.all_gather(keys_values, "seq", axis=0, tiled=True)
    kv_local = seq_idx // group_size
    pair_head = lax.dynamic_slice_in_dim(pair_all, kv_local * HD, HD, axis=2)
    key_head = pair_head[:, 0, :]
    value_head = pair_head[:, 1, :]
    doc_ids = segments
    out_rows = rows_all // n_ten
    block_rows = out_rows // CHUNKS
    pieces = []
    for chunk in range(CHUNKS):
        blocks = [
            attend_rows(query_head, key_head, value_head, doc_ids, part * out_rows + chunk * block_rows, block_rows)
            for part in range(n_ten)
        ]
        chunk_heads = jnp.concatenate(blocks, axis=0)
        gathered = lax.all_gather(chunk_heads, "seq", axis=1, tiled=True)
        projected = jnp.dot(gathered, out_weight, preferred_element_type=jnp.float32)
        pieces.append(lax.psum_scatter(projected, "tensor", scatter_dimension=0, tiled=True))
    summed = jnp.concatenate(pieces, axis=0)
    return (residual.astype(jnp.float32) + summed).astype(jnp.bfloat16)


def solution(mesh):
    placed = (
        P(("dp", "seq"), "tensor"),
        P(("dp", "seq"), None, "tensor"),
        P("tensor", "seq"),
        P(("dp", "tensor"), "seq"),
        P("dp"),
    )
    return jax.shard_map(
        on_device, mesh=mesh, in_specs=placed, out_specs=P(("dp", "tensor"), "seq"), check_vma=False
    )
```

```python
import jax
import jax.numpy as jnp
import numpy as np
from jax import lax
from jax.sharding import PartitionSpec as P

H = 64
KVH = 8
HD = 128
L = 4096


def attend(query_head, key_head, value_head, doc_ids):
    rows_all = query_head.shape[0]
    block_rows = min(512, rows_all)
    score_scale = HD ** (-0.5)
    outputs = []
    for block_index in range(rows_all // block_rows):
        first_row = block_index * block_rows
        key_end = first_row + block_rows
        raw_scores = (
            jnp.einsum(
                "qd,kd->qk",
                query_head[first_row:key_end],
                key_head[:key_end],
                preferred_element_type=jnp.float32,
            )
            * score_scale
        )
        query_pos = first_row + jnp.arange(block_rows)[:, None]
        key_pos = jnp.arange(key_end)[None, :]
        same_doc = doc_ids[first_row:key_end, None] == doc_ids[None, :key_end]
        allowed = (key_pos <= query_pos) & same_doc
        masked = jnp.where(allowed, raw_scores, -1e30)
        highest = jnp.max(masked, axis=-1, keepdims=True)
        exponents = jnp.where(allowed, jnp.exp(masked - highest), 0.0)
        weights = (exponents / jnp.sum(exponents, axis=-1, keepdims=True)).astype(jnp.bfloat16)
        blended = jnp.einsum(
            "qk,kd->qd", weights, value_head[:key_end], preferred_element_type=jnp.float32
        )
        outputs.append(blended.astype(jnp.bfloat16))
    return jnp.concatenate(outputs, axis=0)


def on_device(queries, keys_values, out_weight, residual, segments):
    n_seq = lax.axis_size("seq")
    seq_idx = lax.axis_index("seq")
    tok_dev = queries.shape[0]
    heads_ten = queries.shape[1] // HD
    assert heads_ten == n_seq
    group_size = H // KVH
    head_major = jnp.transpose(queries.reshape(tok_dev, heads_ten, HD), (1, 0, 2))
    query_parts = lax.all_to_all(head_major, "seq", split_axis=0, concat_axis=0, tiled=True)
    query_head = query_parts.reshape(n_seq * tok_dev, HD)
    assert query_head.shape[0] == L
    pair_all = lax.all_gather(keys_values, "seq", axis=0, tiled=True)
    pair_head = lax.dynamic_slice_in_dim(pair_all, (seq_idx // group_size) * HD, HD, axis=2)
    heads_out = attend(query_head, pair_head[:, 0, :], pair_head[:, 1, :], segments)
    gathered = lax.all_gather(heads_out, "seq", axis=1, tiled=True)
    summed = lax.psum_scatter(
        jnp.dot(gathered, out_weight, preferred_element_type=jnp.float32),
        "tensor",
        scatter_dimension=0,
        tiled=True,
    )
    return (residual.astype(jnp.float32) + summed).astype(jnp.bfloat16)


def solution(mesh):
    placed = (
        P(("dp", "seq"), "tensor"),
        P(("dp", "seq"), None, "tensor"),
        P("tensor", "seq"),
        P(("dp", "tensor"), "seq"),
        P("dp"),
    )
    return jax.shard_map(
        on_device, mesh=mesh, in_specs=placed, out_specs=P(("dp", "tensor"), "seq"), check_vma=False
    )
```

```python
import jax
import jax.numpy as jnp
import numpy as np
from jax import lax
from jax.sharding import PartitionSpec as P

H = 64
KVH = 8
HD = 128
L = 4096


def attend(query_head, key_head, value_head, doc_ids):
    rows_all = query_head.shape[0]
    block_rows = min(512, rows_all)
    score_scale = HD ** (-0.5)
    outputs = []
    for block_index in range(rows_all // block_rows):
        first_row = block_index * block_rows
        key_end = first_row + block_rows
        raw_scores = (
            jnp.einsum(
                "qd,kd->qk",
                query_head[first_row:key_end],
                key_head[:key_end],
                preferred_element_type=jnp.float32,
            )
            * score_scale
        )
        query_pos = first_row + jnp.arange(block_rows)[:, None]
        key_pos = jnp.arange(key_end)[None, :]
        same_doc = doc_ids[first_row:key_end, None] == doc_ids[None, :key_end]
        allowed = (key_pos <= query_pos) & same_doc
        masked = jnp.where(allowed, raw_scores, -1e30)
        highest = jnp.max(masked, axis=-1, keepdims=True)
        exponents = jnp.where(allowed, jnp.exp(masked - highest), 0.0)
        weights = (exponents / jnp.sum(exponents, axis=-1, keepdims=True)).astype(jnp.bfloat16)
        blended = jnp.einsum(
            "qk,kd->qd", weights, value_head[:key_end], preferred_element_type=jnp.float32
        )
        outputs.append(blended.astype(jnp.bfloat16))
    return jnp.concatenate(outputs, axis=0)


def on_device(queries, keys_values, out_weight, residual, segments):
    n_seq = lax.axis_size("seq")
    seq_idx = lax.axis_index("seq")
    tok_dev = queries.shape[0]
    heads_ten = queries.shape[1] // HD
    assert heads_ten == n_seq
    group_size = H // KVH
    head_major = jnp.transpose(queries.reshape(tok_dev, heads_ten, HD), (1, 0, 2))
    query_parts = lax.all_to_all(head_major, "seq", split_axis=0, concat_axis=0, tiled=True)
    query_head = query_parts.reshape(n_seq * tok_dev, HD)
    assert query_head.shape[0] == L
    pair_all = lax.all_gather(keys_values, "seq", axis=0, tiled=True)
    pair_head = lax.dynamic_slice_in_dim(pair_all, (seq_idx // group_size) * HD, HD, axis=2)
    heads_out = attend(query_head, pair_head[:, 0, :], pair_head[:, 1, :], segments)
    gathered = lax.all_gather(heads_out, "seq", axis=1, tiled=True)
    summed = lax.psum_scatter(
        jnp.dot(gathered, out_weight, preferred_element_type=jnp.float32).astype(jnp.bfloat16),
        "tensor",
        scatter_dimension=0,
        tiled=True,
    )
    return (residual.astype(jnp.float32) + summed).astype(jnp.bfloat16)


def solution(mesh):
    placed = (
        P(("dp", "seq"), "tensor"),
        P(("dp", "seq"), None, "tensor"),
        P("tensor", "seq"),
        P(("dp", "tensor"), "seq"),
        P("dp"),
    )
    return jax.shard_map(
        on_device, mesh=mesh, in_specs=placed, out_specs=P(("dp", "tensor"), "seq"), check_vma=False
    )
```

```python
import functools
import jax
import jax.numpy as jnp
import numpy as np
from jax import lax
from jax.experimental import pallas as pl
from jax.experimental.pallas import tpu as pltpu
from jax.sharding import PartitionSpec as P

H = 64
KVH = 8
HD = 128
L = 4096


def flash_kernel(starts_ref, q_ref, k_ref, v_ref, segq_ref, segk_ref, o_ref, *, bq, bk):
    qi = pl.program_id(0)
    q = q_ref[...]
    seg_q = segq_ref[...]
    row_pos = qi * bq + lax.broadcasted_iota(jnp.int32, (bq, bk), 0)

    def body(kb, carry):
        m_prev, l_prev, acc_prev = carry
        start = pl.multiple_of(kb * bk, bk)
        k_blk = k_ref[pl.ds(start, bk), :]
        v_blk = v_ref[pl.ds(start, bk), :]
        seg_k = segk_ref[:, pl.ds(start, bk)]
        scores = lax.dot_general(
            q, k_blk, (((1,), (1,)), ((), ())), preferred_element_type=jnp.float32
        ) * (HD ** -0.5)
        col_pos = start + lax.broadcasted_iota(jnp.int32, (bq, bk), 1)
        allowed = (col_pos <= row_pos) & (seg_q == seg_k)
        masked = jnp.where(allowed, scores, -1e30)
        m_new = jnp.maximum(m_prev, jnp.max(masked, axis=1, keepdims=True))
        alpha = jnp.exp(m_prev - m_new)
        probs = jnp.where(allowed, jnp.exp(masked - m_new), 0.0)
        l_new = alpha * l_prev + jnp.sum(probs, axis=1, keepdims=True)
        acc_new = alpha * acc_prev + jnp.dot(
            probs.astype(jnp.bfloat16), v_blk, preferred_element_type=jnp.float32
        )
        return m_new, l_new, acc_new

    init = (
        jnp.full((bq, 1), -1e30, jnp.float32),
        jnp.zeros((bq, 1), jnp.float32),
        jnp.zeros((bq, HD), jnp.float32),
    )
    last = (qi * bq + bq - 1) // bk
    _, l_fin, acc_fin = lax.fori_loop(starts_ref[qi], last + 1, body, init)
    o_ref[...] = (acc_fin / l_fin).astype(o_ref.dtype)


def flash(query_head, key_head, value_head, segments, bq=512, bk=512):
    rows = query_head.shape[0]
    n_q = rows // bq
    first_docs = segments[::bq]
    starts = (jnp.searchsorted(segments, first_docs, side="left") // bk).astype(jnp.int32)
    seg_col = segments.reshape(rows, 1)
    seg_row = segments.reshape(1, rows)
    kernel = functools.partial(flash_kernel, bq=bq, bk=bk)
    return pl.pallas_call(
        kernel,
        out_shape=jax.ShapeDtypeStruct((rows, HD), jnp.bfloat16),
        grid_spec=pltpu.PrefetchScalarGridSpec(
            num_scalar_prefetch=1,
            grid=(n_q,),
            in_specs=[
                pl.BlockSpec((bq, HD), lambda i, s: (i, 0)),
                pl.BlockSpec((rows, HD), lambda i, s: (0, 0)),
                pl.BlockSpec((rows, HD), lambda i, s: (0, 0)),
                pl.BlockSpec((bq, 1), lambda i, s: (i, 0)),
                pl.BlockSpec((1, rows), lambda i, s: (0, 0)),
            ],
            out_specs=pl.BlockSpec((bq, HD), lambda i, s: (i, 0)),
        ),
        compiler_params=pltpu.CompilerParams(dimension_semantics=("arbitrary",)),
    )(starts, query_head, key_head, value_head, seg_col, seg_row)


def on_device(queries, keys_values, out_weight, residual, segments):
    n_seq = lax.axis_size("seq")
    seq_idx = lax.axis_index("seq")
    tok_dev = queries.shape[0]
    heads_ten = queries.shape[1] // HD
    assert heads_ten == n_seq
    group_size = H // KVH
    head_major = jnp.transpose(queries.reshape(tok_dev, heads_ten, HD), (1, 0, 2))
    query_parts = lax.all_to_all(head_major, "seq", split_axis=0, concat_axis=0, tiled=True)
    query_head = query_parts.reshape(n_seq * tok_dev, HD)
    assert query_head.shape[0] == L
    pair_all = lax.all_gather(keys_values, "seq", axis=0, tiled=True)
    pair_head = lax.dynamic_slice_in_dim(pair_all, (seq_idx // group_size) * HD, HD, axis=2)
    heads_out = flash(query_head, pair_head[:, 0, :], pair_head[:, 1, :], segments)
    gathered = lax.all_gather(heads_out, "seq", axis=1, tiled=True)
    summed = lax.psum_scatter(
        jnp.dot(gathered, out_weight, preferred_element_type=jnp.float32).astype(jnp.bfloat16),
        "tensor",
        scatter_dimension=0,
        tiled=True,
    )
    return (residual.astype(jnp.float32) + summed).astype(jnp.bfloat16)


def solution(mesh):
    placed = (
        P(("dp", "seq"), "tensor"),
        P(("dp", "seq"), None, "tensor"),
        P("tensor", "seq"),
        P(("dp", "tensor"), "seq"),
        P("dp"),
    )
    return jax.shard_map(
        on_device, mesh=mesh, in_specs=placed, out_specs=P(("dp", "tensor"), "seq"), check_vma=False
    )
```

```python
import functools
import jax
import jax.numpy as jnp
import numpy as np
from jax import lax
from jax.experimental import pallas as pl
from jax.experimental.pallas import tpu as pltpu
from jax.sharding import PartitionSpec as P

H = 64
KVH = 8
HD = 128
L = 4096


def flash_kernel(starts_ref, q_ref, k_ref, v_ref, segq_ref, segk_ref, o_ref, *, bq, bk):
    qi = pl.program_id(0)
    q = q_ref[...]
    seg_q = segq_ref[...]
    row_pos = qi * bq + lax.broadcasted_iota(jnp.int32, (bq, bk), 0)

    def body(kb, carry):
        m_prev, l_prev, acc_prev = carry
        start = pl.multiple_of(kb * bk, bk)
        k_blk = k_ref[pl.ds(start, bk), :]
        v_blk = v_ref[pl.ds(start, bk), :]
        seg_k = segk_ref[:, pl.ds(start, bk)]
        scores = lax.dot_general(
            q, k_blk, (((1,), (1,)), ((), ())), preferred_element_type=jnp.float32
        ) * (HD ** -0.5)
        col_pos = start + lax.broadcasted_iota(jnp.int32, (bq, bk), 1)
        allowed = (col_pos <= row_pos) & (seg_q == seg_k)
        masked = jnp.where(allowed, scores, -1e30)
        m_new = jnp.maximum(m_prev, jnp.max(masked, axis=1, keepdims=True))
        alpha = jnp.exp(m_prev - m_new)
        probs = jnp.where(allowed, jnp.exp(masked - m_new), 0.0)
        l_new = alpha * l_prev + jnp.sum(probs, axis=1, keepdims=True)
        acc_new = alpha * acc_prev + jnp.dot(
            probs.astype(jnp.bfloat16), v_blk, preferred_element_type=jnp.float32
        )
        return m_new, l_new, acc_new

    init = (
        jnp.full((bq, 1), -1e30, jnp.float32),
        jnp.zeros((bq, 1), jnp.float32),
        jnp.zeros((bq, HD), jnp.float32),
    )
    last = (qi * bq + bq - 1) // bk
    _, l_fin, acc_fin = lax.fori_loop(starts_ref[qi], last + 1, body, init)
    o_ref[...] = (acc_fin / l_fin).astype(o_ref.dtype)


def flash(query_head, key_head, value_head, segments, bq=512, bk=512):
    rows = query_head.shape[0]
    n_q = rows // bq
    first_docs = segments[::bq]
    starts = (jnp.searchsorted(segments, first_docs, side="left") // bk).astype(jnp.int32)
    seg_col = segments.reshape(rows, 1)
    seg_row = segments.reshape(1, rows)
    kernel = functools.partial(flash_kernel, bq=bq, bk=bk)
    return pl.pallas_call(
        kernel,
        out_shape=jax.ShapeDtypeStruct((rows, HD), jnp.bfloat16),
        grid_spec=pltpu.PrefetchScalarGridSpec(
            num_scalar_prefetch=1,
            grid=(n_q,),
            in_specs=[
                pl.BlockSpec((bq, HD), lambda i, s: (i, 0)),
                pl.BlockSpec((rows, HD), lambda i, s: (0, 0)),
                pl.BlockSpec((rows, HD), lambda i, s: (0, 0)),
                pl.BlockSpec((bq, 1), lambda i, s: (i, 0)),
                pl.BlockSpec((1, rows), lambda i, s: (0, 0)),
            ],
            out_specs=pl.BlockSpec((bq, HD), lambda i, s: (i, 0)),
        ),
        compiler_params=pltpu.CompilerParams(dimension_semantics=("arbitrary",)),
    )(starts, query_head, key_head, value_head, seg_col, seg_row)


def on_device(queries, keys_values, out_weight, residual, segments):
    n_core = lax.axis_size("core")
    n_seq = lax.axis_size("z") * n_core
    tok_dev = queries.shape[0]
    heads_ten = queries.shape[1] // HD
    kv_ten = keys_values.shape[2] // HD
    assert heads_ten == n_seq and kv_ten == n_core
    group_size = H // KVH
    order = np.array([group_size * (j % n_core) + j // n_core for j in range(n_seq)], dtype=np.int32)
    head_major = jnp.transpose(queries.reshape(tok_dev, heads_ten, HD), (1, 0, 2))[order]
    query_parts = lax.all_to_all(head_major, ("z", "core"), split_axis=0, concat_axis=0, tiled=True)
    query_head = query_parts.reshape(n_seq * tok_dev, HD)
    assert query_head.shape[0] == L
    pair_split = keys_values.reshape(tok_dev, 2, kv_ten, HD)
    pair_core = lax.all_to_all(pair_split, "core", split_axis=2, concat_axis=0, tiled=True)
    pair_head = lax.all_gather(pair_core, "z", axis=0, tiled=True).reshape(n_seq * tok_dev, 2, HD)
    heads_out = flash(query_head, pair_head[:, 0, :], pair_head[:, 1, :], segments)
    gathered = lax.all_gather(heads_out, ("z", "core"), axis=1, tiled=True)
    weight_rows = out_weight.reshape(heads_ten, HD, out_weight.shape[1])[order].reshape(out_weight.shape)
    summed = lax.psum_scatter(
        jnp.dot(gathered, weight_rows, preferred_element_type=jnp.float32).astype(jnp.bfloat16),
        "tensor",
        scatter_dimension=0,
        tiled=True,
    )
    return (residual.astype(jnp.float32) + summed).astype(jnp.bfloat16)


def solution(mesh):
    n_dp, n_seq, n_ten = (mesh.shape[name] for name in ("dp", "seq", "tensor"))
    sub_mesh = jax.sharding.Mesh(
        mesh.devices.reshape(n_dp, n_seq // 2, 2, n_ten), ("dp", "z", "core", "tensor")
    )
    placed = (
        P(("dp", "z", "core"), "tensor"),
        P(("dp", "z", "core"), None, "tensor"),
        P("tensor", ("z", "core")),
        P(("dp", "tensor"), ("z", "core")),
        P("dp"),
    )
    return jax.shard_map(
        on_device,
        mesh=sub_mesh,
        in_specs=placed,
        out_specs=P(("dp", "tensor"), ("z", "core")),
        check_vma=False,
    )
```

```python
import functools
import jax
import jax.numpy as jnp
import numpy as np
from jax import lax
from jax.experimental import pallas as pl
from jax.experimental.pallas import tpu as pltpu
from jax.sharding import PartitionSpec as P

H = 64
KVH = 8
HD = 128
L = 4096


def flash_kernel(starts_ref, q_ref, k_ref, v_ref, segq_ref, segk_ref, o_ref, *, bq, bk):
    qi = pl.program_id(0)
    q = q_ref[...]
    seg_q = segq_ref[...]
    row_pos = qi * bq + lax.broadcasted_iota(jnp.int32, (bq, bk), 0)

    def body(kb, carry):
        m_prev, l_prev, acc_prev = carry
        start = pl.multiple_of(kb * bk, bk)
        k_blk = k_ref[pl.ds(start, bk), :]
        v_blk = v_ref[pl.ds(start, bk), :]
        seg_k = segk_ref[:, pl.ds(start, bk)]
        scores = lax.dot_general(
            q, k_blk, (((1,), (1,)), ((), ())), preferred_element_type=jnp.float32
        ) * (HD ** -0.5)
        col_pos = start + lax.broadcasted_iota(jnp.int32, (bq, bk), 1)
        allowed = (col_pos <= row_pos) & (seg_q == seg_k)
        masked = jnp.where(allowed, scores, -1e30)
        m_new = jnp.maximum(m_prev, jnp.max(masked, axis=1, keepdims=True))
        alpha = jnp.exp(m_prev - m_new)
        probs = jnp.where(allowed, jnp.exp(masked - m_new), 0.0)
        l_new = alpha * l_prev + jnp.sum(probs, axis=1, keepdims=True)
        acc_new = alpha * acc_prev + jnp.dot(
            probs.astype(jnp.bfloat16), v_blk, preferred_element_type=jnp.float32
        )
        return m_new, l_new, acc_new

    init = (
        jnp.full((bq, 1), -1e30, jnp.float32),
        jnp.zeros((bq, 1), jnp.float32),
        jnp.zeros((bq, HD), jnp.float32),
    )
    last = (qi * bq + bq - 1) // bk
    _, l_fin, acc_fin = lax.fori_loop(starts_ref[qi], last + 1, body, init)
    o_ref[...] = (acc_fin / l_fin).astype(o_ref.dtype)


def flash(query_head, key_head, value_head, segments, bq=512, bk=512):
    rows = query_head.shape[0]
    n_q = rows // bq
    first_docs = segments[::bq]
    starts = (jnp.searchsorted(segments, first_docs, side="left") // bk).astype(jnp.int32)
    seg_col = segments.reshape(rows, 1)
    seg_row = segments.reshape(1, rows)
    kernel = functools.partial(flash_kernel, bq=bq, bk=bk)
    return pl.pallas_call(
        kernel,
        out_shape=jax.ShapeDtypeStruct((rows, HD), jnp.bfloat16),
        grid_spec=pltpu.PrefetchScalarGridSpec(
            num_scalar_prefetch=1,
            grid=(n_q,),
            in_specs=[
                pl.BlockSpec((bq, HD), lambda i, s: (i, 0)),
                pl.BlockSpec((rows, HD), lambda i, s: (0, 0)),
                pl.BlockSpec((rows, HD), lambda i, s: (0, 0)),
                pl.BlockSpec((bq, 1), lambda i, s: (i, 0)),
                pl.BlockSpec((1, rows), lambda i, s: (0, 0)),
            ],
            out_specs=pl.BlockSpec((bq, HD), lambda i, s: (i, 0)),
        ),
        compiler_params=pltpu.CompilerParams(dimension_semantics=("arbitrary",)),
    )(starts, query_head, key_head, value_head, seg_col, seg_row)


def on_device(queries, keys_values, out_weight, residual, segments):
    n_seq = lax.axis_size("seq")
    seq_idx = lax.axis_index("seq")
    tok_dev = queries.shape[0]
    heads_ten = queries.shape[1] // HD
    assert heads_ten == n_seq
    group_size = H // KVH
    head_major = jnp.transpose(queries.reshape(tok_dev, heads_ten, HD), (1, 0, 2))
    query_parts = lax.all_to_all(head_major, "seq", split_axis=0, concat_axis=0, tiled=True)
    query_head = query_parts.reshape(n_seq * tok_dev, HD)
    assert query_head.shape[0] == L
    pair_all = lax.all_gather(keys_values, "seq", axis=0, tiled=True)
    pair_head = lax.dynamic_slice_in_dim(pair_all, (seq_idx // group_size) * HD, HD, axis=2)
    heads_out = flash(query_head, pair_head[:, 0, :], pair_head[:, 1, :], segments)
    gathered = lax.all_gather(heads_out, "seq", axis=1, tiled=True)
    n_ten = lax.axis_size("tensor")
    projected = jnp.dot(gathered, out_weight, preferred_element_type=jnp.float32).astype(jnp.bfloat16)
    blocks = lax.all_to_all(
        projected.reshape(n_ten, projected.shape[0] // n_ten, projected.shape[1]),
        "tensor",
        split_axis=0,
        concat_axis=0,
        tiled=True,
    )
    summed = jnp.sum(blocks.astype(jnp.float32), axis=0)
    return (residual.astype(jnp.float32) + summed).astype(jnp.bfloat16)


def solution(mesh):
    placed = (
        P(("dp", "seq"), "tensor"),
        P(("dp", "seq"), None, "tensor"),
        P("tensor", "seq"),
        P(("dp", "tensor"), "seq"),
        P("dp"),
    )
    return jax.shard_map(
        on_device, mesh=mesh, in_specs=placed, out_specs=P(("dp", "tensor"), "seq"), check_vma=False
    )
```

```python
import functools
import jax
import jax.numpy as jnp
import numpy as np
from jax import lax
from jax.experimental import pallas as pl
from jax.experimental.pallas import tpu as pltpu
from jax.sharding import PartitionSpec as P

H = 64
KVH = 8
HD = 128
L = 4096


def flash_kernel(starts_ref, q_ref, k_ref, v_ref, segq_ref, segk_ref, o_ref, *, bq, bk):
    qi = pl.program_id(0)
    q = q_ref[...]
    seg_q = segq_ref[...]
    row_pos = qi * bq + lax.broadcasted_iota(jnp.int32, (bq, bk), 0)

    def body(kb, carry):
        m_prev, l_prev, acc_prev = carry
        start = pl.multiple_of(kb * bk, bk)
        k_blk = k_ref[pl.ds(start, bk), :]
        v_blk = v_ref[pl.ds(start, bk), :]
        seg_k = segk_ref[:, pl.ds(start, bk)]
        scores = lax.dot_general(
            q, k_blk, (((1,), (1,)), ((), ())), preferred_element_type=jnp.float32
        ) * (HD ** -0.5)
        col_pos = start + lax.broadcasted_iota(jnp.int32, (bq, bk), 1)
        allowed = (col_pos <= row_pos) & (seg_q == seg_k)
        masked = jnp.where(allowed, scores, -1e30)
        m_new = jnp.maximum(m_prev, jnp.max(masked, axis=1, keepdims=True))
        alpha = jnp.exp(m_prev - m_new)
        probs = jnp.where(allowed, jnp.exp(masked - m_new), 0.0)
        l_new = alpha * l_prev + jnp.sum(probs, axis=1, keepdims=True)
        acc_new = alpha * acc_prev + jnp.dot(
            probs.astype(jnp.bfloat16), v_blk, preferred_element_type=jnp.float32
        )
        return m_new, l_new, acc_new

    init = (
        jnp.full((bq, 1), -1e30, jnp.float32),
        jnp.zeros((bq, 1), jnp.float32),
        jnp.zeros((bq, HD), jnp.float32),
    )
    last = (qi * bq + bq - 1) // bk
    _, l_fin, acc_fin = lax.fori_loop(starts_ref[qi], last + 1, body, init)
    o_ref[...] = (acc_fin / l_fin).astype(o_ref.dtype)


def flash(query_head, key_head, value_head, segments, bq=512, bk=512):
    rows = query_head.shape[0]
    n_q = rows // bq
    first_docs = segments[::bq]
    starts = (jnp.searchsorted(segments, first_docs, side="left") // bk).astype(jnp.int32)
    seg_col = segments.reshape(rows, 1)
    seg_row = segments.reshape(1, rows)
    kernel = functools.partial(flash_kernel, bq=bq, bk=bk)
    return pl.pallas_call(
        kernel,
        out_shape=jax.ShapeDtypeStruct((rows, HD), jnp.bfloat16),
        grid_spec=pltpu.PrefetchScalarGridSpec(
            num_scalar_prefetch=1,
            grid=(n_q,),
            in_specs=[
                pl.BlockSpec((bq, HD), lambda i, s: (i, 0)),
                pl.BlockSpec((rows, HD), lambda i, s: (0, 0)),
                pl.BlockSpec((rows, HD), lambda i, s: (0, 0)),
                pl.BlockSpec((bq, 1), lambda i, s: (i, 0)),
                pl.BlockSpec((1, rows), lambda i, s: (0, 0)),
            ],
            out_specs=pl.BlockSpec((bq, HD), lambda i, s: (i, 0)),
        ),
        compiler_params=pltpu.CompilerParams(dimension_semantics=("arbitrary",)),
    )(starts, query_head, key_head, value_head, seg_col, seg_row)


def on_device(queries, keys_values, out_weight, residual, segments):
    n_seq = lax.axis_size("seq")
    n_ten = lax.axis_size("tensor")
    seq_idx = lax.axis_index("seq")
    ten_idx = lax.axis_index("tensor")
    tok_dev = queries.shape[0]
    heads_ten = queries.shape[1] // HD
    assert heads_ten == n_seq
    group_size = H // KVH
    received = [out_weight] + [
        lax.ppermute(out_weight, "tensor", [(j, (j + shift) % n_ten) for j in range(n_ten)])
        for shift in range(1, n_ten)
    ]
    by_shift = jnp.stack(received).reshape(n_ten, n_seq, HD, out_weight.shape[1])
    source = (ten_idx - jnp.arange(n_ten)) % n_ten
    weight_all = jnp.transpose(jnp.take(by_shift, source, axis=0), (1, 0, 2, 3)).reshape(
        n_ten * out_weight.shape[0], out_weight.shape[1]
    )
    head_major = jnp.transpose(queries.reshape(tok_dev, heads_ten, HD), (1, 0, 2))
    query_parts = lax.all_to_all(head_major, "seq", split_axis=0, concat_axis=0, tiled=True)
    query_head = query_parts.reshape(n_seq * tok_dev, HD)
    assert query_head.shape[0] == L
    pair_all = lax.all_gather(keys_values, "seq", axis=0, tiled=True)
    pair_head = lax.dynamic_slice_in_dim(pair_all, (seq_idx // group_size) * HD, HD, axis=2)
    heads_out = flash(query_head, pair_head[:, 0, :], pair_head[:, 1, :], segments)
    out_rows = heads_out.shape[0] // n_ten
    row_parts = lax.all_to_all(heads_out.reshape(n_ten, out_rows, HD), "tensor", split_axis=0, concat_axis=0, tiled=True)
    token_major = jnp.transpose(row_parts, (1, 0, 2))
    gathered = lax.all_gather(token_major, "seq", axis=1, tiled=False).reshape(out_rows, n_seq * n_ten * HD)
    projected = jnp.dot(gathered, weight_all, preferred_element_type=jnp.float32)
    return (residual.astype(jnp.float32) + projected).astype(jnp.bfloat16)


def solution(mesh):
    placed = (
        P(("dp", "seq"), "tensor"),
        P(("dp", "seq"), None, "tensor"),
        P("tensor", "seq"),
        P(("dp", "tensor"), "seq"),
        P("dp"),
    )
    return jax.shard_map(
        on_device, mesh=mesh, in_specs=placed, out_specs=P(("dp", "tensor"), "seq"), check_vma=False
    )
```

```python
import functools
import jax
import jax.numpy as jnp
from jax import lax
from jax.experimental import pallas as pl
from jax.experimental.pallas import tpu as pltpu
from jax.sharding import PartitionSpec as P

H = 64
KVH = 8
HD = 128
L = 4096


def flash_kernel(starts_ref, offset_ref, q_ref, k_ref, v_ref, segq_ref, segk_ref, o_ref, *, bq, bk):
    qi = offset_ref[0] + pl.program_id(0)
    q = q_ref[...]
    seg_q = segq_ref[...]
    row_pos = qi * bq + lax.broadcasted_iota(jnp.int32, (bq, bk), 0)

    def body(kb, carry):
        m_prev, l_prev, acc_prev = carry
        start = pl.multiple_of(kb * bk, bk)
        k_blk = k_ref[pl.ds(start, bk), :]
        v_blk = v_ref[pl.ds(start, bk), :]
        seg_k = segk_ref[:, pl.ds(start, bk)]
        scores = lax.dot_general(
            q, k_blk, (((1,), (1,)), ((), ())), preferred_element_type=jnp.float32
        ) * (HD ** -0.5)
        col_pos = start + lax.broadcasted_iota(jnp.int32, (bq, bk), 1)
        allowed = (col_pos <= row_pos) & (seg_q == seg_k)
        masked = jnp.where(allowed, scores, -1e30)
        m_new = jnp.maximum(m_prev, jnp.max(masked, axis=1, keepdims=True))
        alpha = jnp.exp(m_prev - m_new)
        probs = jnp.where(allowed, jnp.exp(masked - m_new), 0.0)
        l_new = alpha * l_prev + jnp.sum(probs, axis=1, keepdims=True)
        acc_new = alpha * acc_prev + jnp.dot(
            probs.astype(jnp.bfloat16), v_blk, preferred_element_type=jnp.float32
        )
        return m_new, l_new, acc_new

    init = (
        jnp.full((bq, 1), -1e30, jnp.float32),
        jnp.zeros((bq, 1), jnp.float32),
        jnp.zeros((bq, HD), jnp.float32),
    )
    last = (qi * bq + bq - 1) // bk
    _, l_fin, acc_fin = lax.fori_loop(starts_ref[qi], last + 1, body, init)
    o_ref[...] = (acc_fin / l_fin).astype(o_ref.dtype)


def block_starts(segments, bq, bk):
    first_docs = segments[::bq]
    return (jnp.searchsorted(segments, first_docs, side="left") // bk).astype(jnp.int32)


def flash(query_head, key_head, value_head, segments, starts, row_block, rows_out, bq=512, bk=512):
    rows = query_head.shape[0]
    seg_col = segments.reshape(rows, 1)
    seg_row = segments.reshape(1, rows)
    offset = (row_block * (rows_out // bq)).astype(jnp.int32).reshape(1)
    kernel = functools.partial(flash_kernel, bq=bq, bk=bk)
    return pl.pallas_call(
        kernel,
        out_shape=jax.ShapeDtypeStruct((rows_out, HD), jnp.bfloat16),
        grid_spec=pltpu.PrefetchScalarGridSpec(
            num_scalar_prefetch=2,
            grid=(rows_out // bq,),
            in_specs=[
                pl.BlockSpec((bq, HD), lambda i, s, o: (o[0] + i, 0)),
                pl.BlockSpec((rows, HD), lambda i, s, o: (0, 0)),
                pl.BlockSpec((rows, HD), lambda i, s, o: (0, 0)),
                pl.BlockSpec((bq, 1), lambda i, s, o: (o[0] + i, 0)),
                pl.BlockSpec((1, rows), lambda i, s, o: (0, 0)),
            ],
            out_specs=pl.BlockSpec((bq, HD), lambda i, s, o: (i, 0)),
        ),
        compiler_params=pltpu.CompilerParams(dimension_semantics=("arbitrary",)),
    )(starts, offset, query_head, key_head, value_head, seg_col, seg_row)


def layer(queries, keys_values, out_weight, residual, segments):
    n_seq = lax.axis_size("seq")
    n_ten = lax.axis_size("tensor")
    seq_idx = lax.axis_index("seq")
    ten_idx = lax.axis_index("tensor")
    tok_dev = queries.shape[0]
    heads_ten = queries.shape[1] // HD
    assert heads_ten == n_seq
    group_size = H // KVH
    received = [out_weight] + [
        lax.ppermute(out_weight, "tensor", [(j, (j + shift) % n_ten) for j in range(n_ten)])
        for shift in range(1, n_ten)
    ]
    weight_all = jnp.stack(received).reshape(n_ten * out_weight.shape[0], out_weight.shape[1])
    head_major = jnp.transpose(queries.reshape(tok_dev, heads_ten, HD), (1, 0, 2))
    query_parts = lax.all_to_all(head_major, "seq", split_axis=0, concat_axis=0, tiled=True)
    query_head = query_parts.reshape(n_seq * tok_dev, HD)
    assert query_head.shape[0] == L
    pair_all = lax.all_gather(keys_values, "seq", axis=0, tiled=True)
    pair_head = lax.dynamic_slice_in_dim(pair_all, (seq_idx // group_size) * HD, HD, axis=2)
    key_head = pair_head[:, 0, :]
    value_head = pair_head[:, 1, :]
    out_rows = query_head.shape[0] // n_ten
    starts = block_starts(segments, 512, 512)
    by_shift = [None] * n_ten
    for shift in list(range(1, n_ten)) + [0]:
        target = (ten_idx + shift) % n_ten
        block = flash(query_head, key_head, value_head, segments, starts, target, out_rows)
        if shift:
            block = lax.ppermute(block, "tensor", [(j, (j + shift) % n_ten) for j in range(n_ten)])
        by_shift[shift] = block
    token_major = jnp.stack(by_shift, axis=1)
    gathered = lax.all_gather(token_major, "seq", axis=2, tiled=False).reshape(out_rows, n_ten * n_seq * HD)
    projected = jnp.dot(gathered, weight_all, preferred_element_type=jnp.float32)
    return (residual.astype(jnp.float32) + projected).astype(jnp.bfloat16)


def solution(mesh):
    placed = (
        P(("dp", "seq"), "tensor"),
        P(("dp", "seq"), None, "tensor"),
        P("tensor", "seq"),
        P(("dp", "tensor"), "seq"),
        P("dp"),
    )
    return jax.shard_map(
        layer, mesh=mesh, in_specs=placed, out_specs=P(("dp", "tensor"), "seq"), check_vma=False
    )
```

```python
import functools
import jax
import jax.numpy as jnp
from jax import lax
from jax.experimental import pallas as pl
from jax.experimental.pallas import tpu as pltpu
from jax.sharding import PartitionSpec as P

H = 64
KVH = 8
HD = 128
L = 4096


def flash_kernel(starts_ref, q_ref, k_ref, v_ref, segq_ref, segk_ref, o_ref, *, bq, bk):
    qi = pl.program_id(0)
    q = q_ref[...]
    seg_q = segq_ref[...]
    row_pos = qi * bq + lax.broadcasted_iota(jnp.int32, (bq, bk), 0)

    def body(kb, carry):
        m_prev, l_prev, acc_prev = carry
        start = pl.multiple_of(kb * bk, bk)
        k_blk = k_ref[pl.ds(start, bk), :]
        v_blk = v_ref[pl.ds(start, bk), :]
        seg_k = segk_ref[:, pl.ds(start, bk)]
        scores = lax.dot_general(
            q, k_blk, (((1,), (1,)), ((), ())), preferred_element_type=jnp.float32
        ) * (HD ** -0.5)
        col_pos = start + lax.broadcasted_iota(jnp.int32, (bq, bk), 1)
        allowed = (col_pos <= row_pos) & (seg_q == seg_k)
        masked = jnp.where(allowed, scores, -1e30)
        m_new = jnp.maximum(m_prev, jnp.max(masked, axis=1, keepdims=True))
        alpha = jnp.exp(m_prev - m_new)
        probs = jnp.where(allowed, jnp.exp(masked - m_new), 0.0)
        l_new = alpha * l_prev + jnp.sum(probs, axis=1, keepdims=True)
        acc_new = alpha * acc_prev + jnp.dot(
            probs.astype(jnp.bfloat16), v_blk, preferred_element_type=jnp.float32
        )
        return m_new, l_new, acc_new

    init = (
        jnp.full((bq, 1), -1e30, jnp.float32),
        jnp.zeros((bq, 1), jnp.float32),
        jnp.zeros((bq, HD), jnp.float32),
    )
    last = (qi * bq + bq - 1) // bk
    _, l_fin, acc_fin = lax.fori_loop(starts_ref[qi], last + 1, body, init)
    o_ref[...] = (acc_fin / l_fin).astype(o_ref.dtype)


def flash(query_head, key_head, value_head, segments, bq=512, bk=512):
    rows = query_head.shape[0]
    n_q = rows // bq
    first_docs = segments[::bq]
    starts = (jnp.searchsorted(segments, first_docs, side="left") // bk).astype(jnp.int32)
    seg_col = segments.reshape(rows, 1)
    seg_row = segments.reshape(1, rows)
    kernel = functools.partial(flash_kernel, bq=bq, bk=bk)
    return pl.pallas_call(
        kernel,
        out_shape=jax.ShapeDtypeStruct((rows, HD), jnp.bfloat16),
        grid_spec=pltpu.PrefetchScalarGridSpec(
            num_scalar_prefetch=1,
            grid=(n_q,),
            in_specs=[
                pl.BlockSpec((bq, HD), lambda i, s: (i, 0)),
                pl.BlockSpec((rows, HD), lambda i, s: (0, 0)),
                pl.BlockSpec((rows, HD), lambda i, s: (0, 0)),
                pl.BlockSpec((bq, 1), lambda i, s: (i, 0)),
                pl.BlockSpec((1, rows), lambda i, s: (0, 0)),
            ],
            out_specs=pl.BlockSpec((bq, HD), lambda i, s: (i, 0)),
        ),
        compiler_params=pltpu.CompilerParams(dimension_semantics=("arbitrary",)),
    )(starts, query_head, key_head, value_head, seg_col, seg_row)


def layer(queries, keys_values, out_weight, residual, segments):
    n_core = lax.axis_size("core")
    n_z = lax.axis_size("z")
    n_seq = n_z * n_core
    n_ten = lax.axis_size("tensor")
    core_idx = lax.axis_index("core")
    seq_idx = lax.axis_index("z") * n_core + core_idx
    ten_idx = lax.axis_index("tensor")
    tok_dev = queries.shape[0]
    heads_ten = queries.shape[1] // HD
    assert heads_ten == n_seq
    group_size = H // KVH
    received = [out_weight] + [
        lax.ppermute(out_weight, "tensor", [(j, (j + shift) % n_ten) for j in range(n_ten)])
        for shift in range(1, n_ten)
    ]
    by_shift = jnp.stack(received)
    source = (ten_idx - jnp.arange(n_ten)) % n_ten
    weight_all = jnp.take(by_shift, source, axis=0).reshape(n_ten * out_weight.shape[0], out_weight.shape[1])
    head_major = jnp.transpose(queries.reshape(tok_dev, heads_ten, HD), (1, 0, 2))
    query_parts = lax.all_to_all(head_major, ("z", "core"), split_axis=0, concat_axis=0, tiled=True)
    query_head = query_parts.reshape(n_seq * tok_dev, HD)
    assert query_head.shape[0] == L
    pair_all = lax.all_gather(keys_values, ("z", "core"), axis=0, tiled=True)
    pair_head = lax.dynamic_slice_in_dim(pair_all, (seq_idx // group_size) * HD, HD, axis=2)
    heads_out = flash(query_head, pair_head[:, 0, :], pair_head[:, 1, :], segments)
    out_rows = heads_out.shape[0] // n_ten
    row_parts = lax.all_to_all(heads_out.reshape(n_ten, out_rows, HD), "tensor", split_axis=0, concat_axis=0, tiled=True)
    token_major = jnp.transpose(row_parts, (1, 0, 2))
    own = lax.all_gather(token_major, "z", axis=2, tiled=False)
    sibling = lax.ppermute(own, "core", [(j, (j + 1) % n_core) for j in range(n_core)])
    weight_parts = weight_all.reshape(n_ten, n_z, n_core, HD, weight_all.shape[1])
    weight_own = lax.dynamic_index_in_dim(weight_parts, core_idx, axis=2, keepdims=False)
    weight_sib = lax.dynamic_index_in_dim(weight_parts, (core_idx + 1) % n_core, axis=2, keepdims=False)
    features = n_ten * n_z * HD
    projected = jnp.dot(
        own.reshape(out_rows, features), weight_own.reshape(features, -1), preferred_element_type=jnp.float32
    ) + jnp.dot(
        sibling.reshape(out_rows, features), weight_sib.reshape(features, -1), preferred_element_type=jnp.float32
    )
    return (residual.astype(jnp.float32) + projected).astype(jnp.bfloat16)


def solution(mesh):
    n_dp, n_seq, n_ten = (mesh.shape[name] for name in ("dp", "seq", "tensor"))
    sub_mesh = jax.sharding.Mesh(
        mesh.devices.reshape(n_dp, n_seq // 2, 2, n_ten), ("dp", "z", "core", "tensor")
    )
    placed = (
        P(("dp", "z", "core"), "tensor"),
        P(("dp", "z", "core"), None, "tensor"),
        P("tensor", ("z", "core")),
        P(("dp", "tensor"), ("z", "core")),
        P("dp"),
    )
    return jax.shard_map(
        layer,
        mesh=sub_mesh,
        in_specs=placed,
        out_specs=P(("dp", "tensor"), ("z", "core")),
        check_vma=False,
    )
```

```python
import functools
import jax
import jax.numpy as jnp
from jax import lax
from jax.experimental import pallas as pl
from jax.experimental.pallas import tpu as pltpu
from jax.sharding import PartitionSpec as P

H = 64
KVH = 8
HD = 128
L = 4096


def flash_kernel(starts_ref, q_ref, k_ref, v_ref, segq_ref, segk_ref, o_ref, *, bq, bk):
    qi = pl.program_id(0)
    q = q_ref[...]
    seg_q = segq_ref[...]
    row_pos = qi * bq + lax.broadcasted_iota(jnp.int32, (bq, bk), 0)

    def body(kb, carry):
        m_prev, l_prev, acc_prev = carry
        start = pl.multiple_of(kb * bk, bk)
        k_blk = k_ref[pl.ds(start, bk), :]
        v_blk = v_ref[pl.ds(start, bk), :]
        seg_k = segk_ref[:, pl.ds(start, bk)]
        scores = lax.dot_general(
            q, k_blk, (((1,), (1,)), ((), ())), preferred_element_type=jnp.float32
        ) * (HD ** -0.5)
        col_pos = start + lax.broadcasted_iota(jnp.int32, (bq, bk), 1)
        allowed = (col_pos <= row_pos) & (seg_q == seg_k)
        masked = jnp.where(allowed, scores, -1e30)
        m_new = jnp.maximum(m_prev, jnp.max(masked, axis=1, keepdims=True))
        alpha = jnp.exp(m_prev - m_new)
        probs = jnp.where(allowed, jnp.exp(masked - m_new), 0.0)
        l_new = alpha * l_prev + jnp.sum(probs, axis=1, keepdims=True)
        acc_new = alpha * acc_prev + jnp.dot(
            probs.astype(jnp.bfloat16), v_blk, preferred_element_type=jnp.float32
        )
        return m_new, l_new, acc_new

    init = (
        jnp.full((bq, 1), -1e30, jnp.float32),
        jnp.zeros((bq, 1), jnp.float32),
        jnp.zeros((bq, HD), jnp.float32),
    )
    last = (qi * bq + bq - 1) // bk
    _, l_fin, acc_fin = lax.fori_loop(starts_ref[qi], last + 1, body, init)
    o_ref[...] = (acc_fin / l_fin).astype(o_ref.dtype)


def flash(query_head, key_head, value_head, segments, bq=512, bk=1024):
    rows = query_head.shape[0]
    n_q = rows // bq
    first_docs = segments[::bq]
    starts = (jnp.searchsorted(segments, first_docs, side="left") // bk).astype(jnp.int32)
    seg_col = segments.reshape(rows, 1)
    seg_row = segments.reshape(1, rows)
    kernel = functools.partial(flash_kernel, bq=bq, bk=bk)
    return pl.pallas_call(
        kernel,
        out_shape=jax.ShapeDtypeStruct((rows, HD), jnp.bfloat16),
        grid_spec=pltpu.PrefetchScalarGridSpec(
            num_scalar_prefetch=1,
            grid=(n_q,),
            in_specs=[
                pl.BlockSpec((bq, HD), lambda i, s: (i, 0)),
                pl.BlockSpec((rows, HD), lambda i, s: (0, 0)),
                pl.BlockSpec((rows, HD), lambda i, s: (0, 0)),
                pl.BlockSpec((bq, 1), lambda i, s: (i, 0)),
                pl.BlockSpec((1, rows), lambda i, s: (0, 0)),
            ],
            out_specs=pl.BlockSpec((bq, HD), lambda i, s: (i, 0)),
        ),
        compiler_params=pltpu.CompilerParams(dimension_semantics=("arbitrary",)),
    )(starts, query_head, key_head, value_head, seg_col, seg_row)


def layer(queries, keys_values, out_weight, residual, segments):
    n_seq = lax.axis_size("seq")
    n_ten = lax.axis_size("tensor")
    seq_idx = lax.axis_index("seq")
    ten_idx = lax.axis_index("tensor")
    tok_dev = queries.shape[0]
    heads_ten = queries.shape[1] // HD
    assert heads_ten == n_seq
    group_size = H // KVH
    received = [out_weight] + [
        lax.ppermute(out_weight, "tensor", [(j, (j + shift) % n_ten) for j in range(n_ten)])
        for shift in range(1, n_ten)
    ]
    by_shift = jnp.stack(received)
    source = (ten_idx - jnp.arange(n_ten)) % n_ten
    weight_all = jnp.take(by_shift, source, axis=0).reshape(n_ten * out_weight.shape[0], out_weight.shape[1])
    head_major = jnp.transpose(queries.reshape(tok_dev, heads_ten, HD), (1, 0, 2))
    query_parts = lax.all_to_all(head_major, "seq", split_axis=0, concat_axis=0, tiled=True)
    query_head = query_parts.reshape(n_seq * tok_dev, HD)
    assert query_head.shape[0] == L
    pair_all = lax.all_gather(keys_values, "seq", axis=0, tiled=True)
    pair_head = lax.dynamic_slice_in_dim(pair_all, (seq_idx // group_size) * HD, HD, axis=2)
    heads_out = flash(query_head, pair_head[:, 0, :], pair_head[:, 1, :], segments)
    out_rows = heads_out.shape[0] // n_ten
    row_parts = lax.all_to_all(heads_out.reshape(n_ten, out_rows, HD), "tensor", split_axis=0, concat_axis=0, tiled=True)
    token_major = jnp.transpose(row_parts, (1, 0, 2))
    gathered = lax.all_gather(token_major, "seq", axis=2, tiled=False).reshape(out_rows, n_ten * n_seq * HD)
    projected = jnp.dot(gathered, weight_all, preferred_element_type=jnp.float32)
    return (residual.astype(jnp.float32) + projected).astype(jnp.bfloat16)


def solution(mesh):
    placed = (
        P(("dp", "seq"), "tensor"),
        P(("dp", "seq"), None, "tensor"),
        P("tensor", "seq"),
        P(("dp", "tensor"), "seq"),
        P("dp"),
    )
    return jax.shard_map(layer, mesh=mesh, in_specs=placed, out_specs=P(("dp", "tensor"), "seq"), check_vma=False)
```

```python
import functools
import jax
import jax.numpy as jnp
from jax import lax
from jax.experimental import pallas as pl
from jax.experimental.pallas import tpu as pltpu
from jax.sharding import PartitionSpec as P

H = 64
KVH = 8
HD = 128
L = 4096


def flash_kernel(starts_ref, head_ref, q_ref, k_ref, v_ref, segq_ref, segk_ref, o_ref, *, bq, bk):
    qi = pl.program_id(0)
    q = q_ref[...]
    seg_q = segq_ref[...]
    row_pos = qi * bq + lax.broadcasted_iota(jnp.int32, (bq, bk), 0)

    def body(kb, carry):
        m_prev, l_prev, acc_prev = carry
        start = pl.multiple_of(kb * bk, bk)
        k_blk = k_ref[pl.ds(start, bk), :]
        v_blk = v_ref[pl.ds(start, bk), :]
        seg_k = segk_ref[:, pl.ds(start, bk)]
        scores = lax.dot_general(
            q, k_blk, (((1,), (1,)), ((), ())), preferred_element_type=jnp.float32
        ) * (HD ** -0.5)
        col_pos = start + lax.broadcasted_iota(jnp.int32, (bq, bk), 1)
        allowed = (col_pos <= row_pos) & (seg_q == seg_k)
        masked = jnp.where(allowed, scores, -1e30)
        m_new = jnp.maximum(m_prev, jnp.max(masked, axis=1, keepdims=True))
        alpha = jnp.exp(m_prev - m_new)
        probs = jnp.where(allowed, jnp.exp(masked - m_new), 0.0)
        l_new = alpha * l_prev + jnp.sum(probs, axis=1, keepdims=True)
        acc_new = alpha * acc_prev + jnp.dot(
            probs.astype(jnp.bfloat16), v_blk, preferred_element_type=jnp.float32
        )
        return m_new, l_new, acc_new

    init = (
        jnp.full((bq, 1), -1e30, jnp.float32),
        jnp.zeros((bq, 1), jnp.float32),
        jnp.zeros((bq, HD), jnp.float32),
    )
    last = (qi * bq + bq - 1) // bk
    _, l_fin, acc_fin = lax.fori_loop(starts_ref[qi], last + 1, body, init)
    o_ref[...] = (acc_fin / l_fin).astype(o_ref.dtype)


def flash(query_head, pair_all, kv_head, segments, bq=512, bk=512):
    rows = query_head.shape[0]
    n_q = rows // bq
    first_docs = segments[::bq]
    starts = (jnp.searchsorted(segments, first_docs, side="left") // bk).astype(jnp.int32)
    seg_col = segments.reshape(rows, 1)
    seg_row = segments.reshape(1, rows)
    kernel = functools.partial(flash_kernel, bq=bq, bk=bk)
    return pl.pallas_call(
        kernel,
        out_shape=jax.ShapeDtypeStruct((rows, HD), jnp.bfloat16),
        grid_spec=pltpu.PrefetchScalarGridSpec(
            num_scalar_prefetch=2,
            grid=(n_q,),
            in_specs=[
                pl.BlockSpec((bq, HD), lambda i, s, h: (i, 0)),
                pl.BlockSpec((None, rows, HD), lambda i, s, h: (0, 0, h[0])),
                pl.BlockSpec((None, rows, HD), lambda i, s, h: (1, 0, h[0])),
                pl.BlockSpec((bq, 1), lambda i, s, h: (i, 0)),
                pl.BlockSpec((1, rows), lambda i, s, h: (0, 0)),
            ],
            out_specs=pl.BlockSpec((bq, HD), lambda i, s, h: (i, 0)),
        ),
        compiler_params=pltpu.CompilerParams(dimension_semantics=("arbitrary",)),
    )(starts, kv_head, query_head, pair_all, pair_all, seg_col, seg_row)


def layer(queries, keys_values, out_weight, residual, segments):
    n_seq = lax.axis_size("seq")
    n_ten = lax.axis_size("tensor")
    seq_idx = lax.axis_index("seq")
    ten_idx = lax.axis_index("tensor")
    tok_dev = queries.shape[0]
    heads_ten = queries.shape[1] // HD
    assert heads_ten == n_seq
    group_size = H // KVH
    received = [out_weight] + [
        lax.ppermute(out_weight, "tensor", [(j, (j + shift) % n_ten) for j in range(n_ten)])
        for shift in range(1, n_ten)
    ]
    by_shift = jnp.stack(received)
    source = (ten_idx - jnp.arange(n_ten)) % n_ten
    weight_all = jnp.take(by_shift, source, axis=0).reshape(n_ten * out_weight.shape[0], out_weight.shape[1])
    head_major = jnp.transpose(queries.reshape(tok_dev, heads_ten, HD), (1, 0, 2))
    query_parts = lax.all_to_all(head_major, "seq", split_axis=0, concat_axis=0, tiled=True)
    query_head = query_parts.reshape(n_seq * tok_dev, HD)
    assert query_head.shape[0] == L
    pair_major = jnp.transpose(keys_values, (1, 0, 2))
    pair_all = lax.all_gather(pair_major, "seq", axis=1, tiled=True)
    kv_head = (seq_idx // group_size).astype(jnp.int32).reshape(1)
    heads_out = flash(query_head, pair_all, kv_head, segments)
    out_rows = heads_out.shape[0] // n_ten
    row_parts = lax.all_to_all(heads_out.reshape(n_ten, out_rows, HD), "tensor", split_axis=0, concat_axis=0, tiled=True)
    token_major = jnp.transpose(row_parts, (1, 0, 2))
    gathered = lax.all_gather(token_major, "seq", axis=2, tiled=False).reshape(out_rows, n_ten * n_seq * HD)
    projected = jnp.dot(gathered, weight_all, preferred_element_type=jnp.float32)
    return (residual.astype(jnp.float32) + projected).astype(jnp.bfloat16)


def solution(mesh):
    placed = (
        P(("dp", "seq"), "tensor"),
        P(("dp", "seq"), None, "tensor"),
        P("tensor", "seq"),
        P(("dp", "tensor"), "seq"),
        P("dp"),
    )
    return jax.shard_map(layer, mesh=mesh, in_specs=placed, out_specs=P(("dp", "tensor"), "seq"), check_vma=False)
```

```python
import functools
import jax
import jax.numpy as jnp
from jax import lax
from jax.experimental import pallas as pl
from jax.experimental.pallas import tpu as pltpu
from jax.sharding import PartitionSpec as P

H = 64
KVH = 8
HD = 128
L = 4096


def flash_kernel(starts_ref, head_ref, q_ref, k_ref, v_ref, segq_ref, segk_ref, o_ref, *, bq, bk):
    qi = pl.program_id(0)
    q = q_ref[...]
    seg_q = segq_ref[...]
    row_pos = qi * bq + lax.broadcasted_iota(jnp.int32, (bq, bk), 0)

    def body(kb, carry, causal=False):
        m_prev, l_prev, acc_prev = carry
        start = pl.multiple_of(kb * bk, bk)
        k_blk = k_ref[pl.ds(start, bk), :]
        v_blk = v_ref[pl.ds(start, bk), :]
        seg_k = segk_ref[:, pl.ds(start, bk)]
        scores = lax.dot_general(
            q, k_blk, (((1,), (1,)), ((), ())), preferred_element_type=jnp.float32
        ) * (HD ** -0.5)
        allowed = seg_q == seg_k
        if causal:
            col_pos = start + lax.broadcasted_iota(jnp.int32, (bq, bk), 1)
            allowed = allowed & (col_pos <= row_pos)
        masked = jnp.where(allowed, scores, -1e30)
        m_new = jnp.maximum(m_prev, jnp.max(masked, axis=1, keepdims=True))
        alpha = jnp.exp(m_prev - m_new)
        probs = jnp.where(allowed, jnp.exp(masked - m_new), 0.0)
        l_new = alpha * l_prev + jnp.sum(probs, axis=1, keepdims=True)
        acc_new = alpha * acc_prev + jnp.dot(
            probs.astype(jnp.bfloat16), v_blk, preferred_element_type=jnp.float32
        )
        return m_new, l_new, acc_new

    init = (
        jnp.full((bq, 1), -1e30, jnp.float32),
        jnp.zeros((bq, 1), jnp.float32),
        jnp.zeros((bq, HD), jnp.float32),
    )
    assert bq == bk
    carry = lax.fori_loop(starts_ref[qi], qi, body, init)
    _, l_fin, acc_fin = body(qi, carry, causal=True)
    o_ref[...] = (acc_fin / l_fin).astype(o_ref.dtype)


def flash(query_head, pair_all, kv_head, segments, bq=512, bk=512):
    rows = query_head.shape[0]
    n_q = rows // bq
    first_docs = segments[::bq]
    starts = (jnp.searchsorted(segments, first_docs, side="left") // bk).astype(jnp.int32)
    seg_col = segments.reshape(rows, 1)
    seg_row = segments.reshape(1, rows)
    kernel = functools.partial(flash_kernel, bq=bq, bk=bk)
    return pl.pallas_call(
        kernel,
        out_shape=jax.ShapeDtypeStruct((rows, HD), jnp.bfloat16),
        grid_spec=pltpu.PrefetchScalarGridSpec(
            num_scalar_prefetch=2,
            grid=(n_q,),
            in_specs=[
                pl.BlockSpec((bq, HD), lambda i, s, h: (i, 0)),
                pl.BlockSpec((None, rows, HD), lambda i, s, h: (0, 0, h[0])),
                pl.BlockSpec((None, rows, HD), lambda i, s, h: (1, 0, h[0])),
                pl.BlockSpec((bq, 1), lambda i, s, h: (i, 0)),
                pl.BlockSpec((1, rows), lambda i, s, h: (0, 0)),
            ],
            out_specs=pl.BlockSpec((bq, HD), lambda i, s, h: (i, 0)),
        ),
        compiler_params=pltpu.CompilerParams(dimension_semantics=("arbitrary",)),
    )(starts, kv_head, query_head, pair_all, pair_all, seg_col, seg_row)


def layer(queries, keys_values, out_weight, residual, segments):
    n_seq = lax.axis_size("seq")
    n_ten = lax.axis_size("tensor")
    seq_idx = lax.axis_index("seq")
    ten_idx = lax.axis_index("tensor")
    tok_dev = queries.shape[0]
    heads_ten = queries.shape[1] // HD
    assert heads_ten == n_seq
    group_size = H // KVH
    received = [out_weight] + [
        lax.ppermute(out_weight, "tensor", [(j, (j + shift) % n_ten) for j in range(n_ten)])
        for shift in range(1, n_ten)
    ]
    by_shift = jnp.stack(received)
    source = (ten_idx - jnp.arange(n_ten)) % n_ten
    weight_all = jnp.take(by_shift, source, axis=0).reshape(n_ten * out_weight.shape[0], out_weight.shape[1])
    head_major = jnp.transpose(queries.reshape(tok_dev, heads_ten, HD), (1, 0, 2))
    query_parts = lax.all_to_all(head_major, "seq", split_axis=0, concat_axis=0, tiled=True)
    query_head = query_parts.reshape(n_seq * tok_dev, HD)
    assert query_head.shape[0] == L
    pair_major = jnp.transpose(keys_values, (1, 0, 2))
    pair_all = lax.all_gather(pair_major, "seq", axis=1, tiled=True)
    kv_head = (seq_idx // group_size).astype(jnp.int32).reshape(1)
    heads_out = flash(query_head, pair_all, kv_head, segments)
    out_rows = heads_out.shape[0] // n_ten
    row_parts = lax.all_to_all(heads_out.reshape(n_ten, out_rows, HD), "tensor", split_axis=0, concat_axis=0, tiled=True)
    token_major = jnp.transpose(row_parts, (1, 0, 2))
    gathered = lax.all_gather(token_major, "seq", axis=2, tiled=False).reshape(out_rows, n_ten * n_seq * HD)
    projected = jnp.dot(gathered, weight_all, preferred_element_type=jnp.float32)
    return (residual.astype(jnp.float32) + projected).astype(jnp.bfloat16)


def solution(mesh):
    placed = (
        P(("dp", "seq"), "tensor"),
        P(("dp", "seq"), None, "tensor"),
        P("tensor", "seq"),
        P(("dp", "tensor"), "seq"),
        P("dp"),
    )
    return jax.shard_map(layer, mesh=mesh, in_specs=placed, out_specs=P(("dp", "tensor"), "seq"), check_vma=False)
```
